512 devices in a mesh: grp: 4 (over x), dev: 128 (over y, z, core).
Axes of the slice: x: 4, y: 8, z: 8, core: 2. Of those that a mesh axis runs over, the one named last changes fastest.
Arguments:
- queries: bfloat16 [131072, 768], P(('grp', 'dev')), parts along dimension 0, may hold values from -10 to 10
- keys: bfloat16 [131072, 384], P(('grp', 'dev')), parts along dimension 0, may hold values from -10 to 10
- values: bfloat16 [131072, 384], P(('grp', 'dev')), parts along dimension 0, may hold values from -6 to 6
- deal_index: int32 [131072], P(('grp', 'dev')), parts along dimension 0, may hold values from 0 to 32767, as said below
- segments: int32 [512, 256], P(('grp', 'dev')), parts along dimension 0, may hold values from 0 to 3, as said below
- page_owner: int32 [512, 128], P(('grp', 'dev')), parts along dimension 0, may hold values from 0 to 127, as said below
Outputs:
- attended: bfloat16 [131072, 768], P(('grp', 'dev')), parts along dimension 0
- cache: bfloat16 [131072, 768], P(('grp', 'dev')), parts along dimension 0
The draws below stay inside these ranges and needn't reach their ends.
There are 4 independent parts, one for each index of `grp`. The reference program is written for one: setup_inputs(seed, part) draws one part's arguments, and reference() takes and returns one part's arrays. A program takes and returns all parts, laid end to end along the dimension named above; each array names one. Nothing has to cross between parts.
Inputs may be any that keep to these rules, and one draw needn't show every extreme that they name: Each dealt row once; a token at row i of its arrival device has deal_index // 256 = i // 2. `segments`: along a device's rows the numbers never fall, each of 0 to 3 appears, and each request holds 32 rows or more. `page_owner`: every row and every column names each device once.
All inputs are finite; a program needn't handle non-finite values.
Results may differ from the reference program's by a relative error of at most 0.0061.
Values may be sent and summed in bfloat16 or wider, within the bound.
No kernel may reach another device: no remote copies, remote signals or barrier semaphores. Data moves between devices by JAX's collectives and lax.ppermute only.
A program may use at most 64 MiB of HBM per device.

```python
import math
import jax
import jax.numpy as jnp
from jax import lax

HEAD_SIZE = 96
QUERY_HEAD_COUNT = 8
KEY_VALUE_HEADS = 4
DEVICE_TOKENS = 256
REQS = 4
PART_TOKENS = 32768
KW = 384


def deal_permutation(key):
    device_count = PART_TOKENS // DEVICE_TOKENS
    page_rows = DEVICE_TOKENS // device_count

    def one_order(order_key):
        return jax.random.permutation(order_key, DEVICE_TOKENS).astype(jnp.int32)
    orders = jax.vmap(one_order)(jax.random.split(jax.random.fold_in(key, 11), device_count))
    blocks = orders.reshape(device_count, device_count, page_rows).transpose(1, 0, 2)
    offsets = (jnp.arange(device_count, dtype=jnp.int32) * DEVICE_TOKENS)[None, :, None]
    return (blocks + offsets).reshape(PART_TOKENS)


def draw_deal_index(key, part):
    return deal_permutation(key)


def draw_segments(key, part):
    device_count = PART_TOKENS // DEVICE_TOKENS
    least_rows = min(128, DEVICE_TOKENS // (2 * REQS))
    spare = DEVICE_TOKENS - REQS * least_rows

    def one_row(row_key):
        picked = jnp.sort(jax.random.permutation(row_key, spare + REQS - 1)[:REQS - 1].astype(jnp.int32))
        rank = jnp.arange(REQS - 1, dtype=jnp.int32)
        cuts = picked - rank + (rank + 1) * least_rows
        counter = jnp.arange(DEVICE_TOKENS, dtype=jnp.int32)
        return jnp.sum((counter[:, None] >= cuts[None, :]).astype(jnp.int32), axis=1)
    return jax.vmap(one_row)(jax.random.split(jax.random.fold_in(key, 13), device_count))


def draw_page_owner(key, part):
    device_count = PART_TOKENS // DEVICE_TOKENS
    first = jax.random.permutation(jax.random.fold_in(key, 31), device_count).astype(jnp.int32)
    second = jax.random.permutation(jax.random.fold_in(key, 37), device_count).astype(jnp.int32)
    third = jax.random.permutation(jax.random.fold_in(key, 41), device_count).astype(jnp.int32)
    return first[(second[:, None] + third[None, :]) % device_count]


def draw_queries(key, part):
    device_count = PART_TOKENS // DEVICE_TOKENS
    offset_base = jnp.clip(jax.random.normal(jax.random.fold_in(key, 19), (device_count, DEVICE_TOKENS, QUERY_HEAD_COUNT, HEAD_SIZE), jnp.float32), -4.0, 4.0)
    return offset_base.reshape(PART_TOKENS, QUERY_HEAD_COUNT * HEAD_SIZE)[deal_permutation(key)].astype(jnp.bfloat16)


def draw_keys(key, part):
    device_count = PART_TOKENS // DEVICE_TOKENS
    offset_base = jnp.clip(jax.random.normal(jax.random.fold_in(key, 23), (device_count, DEVICE_TOKENS, KEY_VALUE_HEADS, HEAD_SIZE), jnp.float32), -4.0, 4.0)
    return offset_base.reshape(PART_TOKENS, KEY_VALUE_HEADS * HEAD_SIZE)[deal_permutation(key)].astype(jnp.bfloat16)


def levels(rng, extent, shards, low, top_value):
    def one(dim, shards_of):
        heights = jax.random.uniform(jax.random.fold_in(jax.random.fold_in(rng, 6), dim), (shards_of,), jnp.float32, low / len(shards), top_value / len(shards))
        return jnp.repeat(jnp.exp(heights), extent[dim] // shards_of).reshape((-1,) + (1,) * (len(extent) - dim - 1))

    level = one(*shards[0])
    for cut in shards[1:]:
        level = level * one(*cut)
    return level


def centred(stream_key, extent, scale, bound, cuts=(), held_as=jnp.bfloat16):
    values = scale * jax.random.normal(stream_key, extent, jnp.float32)
    if cuts:
        values = values * levels(stream_key, extent, cuts, -0.22, 0.18)
    return jnp.clip(values, -bound, bound).astype(held_as)


def setup_inputs(seed: int = 0, part: int = 0) -> dict:
    arg_keys = jax.random.split(jax.random.key(seed), 7)
    part_keys = jax.random.split(jax.random.fold_in(arg_keys[6], part), 7)
    return {
        "queries": draw_queries(jax.random.fold_in(jax.random.fold_in(arg_keys[6], part), 71), part),
        "keys": draw_keys(jax.random.fold_in(jax.random.fold_in(arg_keys[6], part), 71), part),
        "values": centred(part_keys[2], (PART_TOKENS, KW), 1.0, 6.0, ((0, 128),)),
        "deal_index": draw_deal_index(jax.random.fold_in(jax.random.fold_in(arg_keys[6], part), 71), part),
        "segments": draw_segments(jax.random.fold_in(jax.random.fold_in(arg_keys[6], part), 71), part),
        "page_owner": draw_page_owner(jax.random.fold_in(jax.random.fold_in(arg_keys[6], part), 71), part),
    }


ROPE_BASE = 100000.0
NEG_FILL = -1e+30

def positions_of(request_labels):
    row_width = request_labels.shape[0]
    counter = jnp.arange(row_width, dtype=jnp.int32)
    boundary = jnp.concatenate([jnp.ones((1,), jnp.bool_), request_labels[1:] != request_labels[:-1]])
    starts = lax.cummax(jnp.where(boundary, counter, jnp.zeros_like(counter)), axis=0)
    return counter - starts

def apply_rotary(features, token_positions, head_count):
    head_depth = features.shape[1] // head_count
    half_depth = head_depth // 2
    freqs = ROPE_BASE ** (-2.0 * jnp.arange(half_depth, dtype=jnp.float32) / head_depth)
    angles = token_positions.astype(jnp.float32)[:, None] * freqs[None, :]
    cosine = jnp.cos(angles)[:, None, :]
    sine = jnp.sin(angles)[:, None, :]
    split_heads = features.astype(jnp.float32).reshape(features.shape[0], head_count, head_depth)
    first = split_heads[..., :half_depth]
    second = split_heads[..., half_depth:]
    turned = jnp.concatenate([first * cosine - second * sine, second * cosine + first * sine], axis=-1)
    return turned.reshape(features.shape).astype(jnp.bfloat16)

def attend_heads(query_turned, query_rows, key_turned, value_matrix, request_labels, kv_heads):
    row_total = query_turned.shape[0]
    key_total = key_turned.shape[0]
    head_depth = key_turned.shape[1] // kv_heads
    group_size = query_turned.shape[1] // (kv_heads * head_depth)
    query_heads = query_turned.reshape(row_total, kv_heads, group_size, head_depth).transpose(1, 0, 2, 3)
    key_heads = key_turned.reshape(key_total, kv_heads, head_depth).transpose(1, 0, 2)
    value_heads = value_matrix.reshape(key_total, kv_heads, head_depth).transpose(1, 0, 2)
    key_index = jnp.arange(key_total, dtype=jnp.int32)
    allowed = (request_labels[query_rows][:, None] == request_labels[None, :]) & (key_index[None, :] <= query_rows[:, None])
    logit_scale = 1.0 / math.sqrt(head_depth)

    def one_head(operands):
        query_slice, key_slice, value_slice = operands
        attention_logits = jnp.einsum('qhs,bs->hqb', query_slice.astype(jnp.float32), key_slice.astype(jnp.float32)) * logit_scale
        attention_logits = jnp.where(allowed[None], attention_logits, NEG_FILL)
        highest = lax.optimization_barrier(jnp.max(attention_logits, axis=-1, keepdims=True))
        expo = jnp.exp(attention_logits - highest)
        attention_weights = (expo / lax.optimization_barrier(jnp.sum(expo, axis=-1, keepdims=True))).astype(jnp.bfloat16)
        attention_weights = lax.optimization_barrier(attention_weights).astype(jnp.float32)
        return jnp.einsum('vjn,ne->jve', attention_weights, value_slice.astype(jnp.float32))
    output_rows = lax.map(one_head, (query_heads, key_heads, value_heads))
    return output_rows.transpose(1, 0, 2, 3).reshape(row_total, -1).astype(jnp.bfloat16)

def reference(queries, keys, values, deal_index, segments, page_owner):
    device_count = segments.shape[0]
    row_count = segments.shape[1]
    page_rows = row_count // device_count
    token_total = queries.shape[0]
    source_row = jnp.zeros((token_total,), jnp.int32).at[deal_index].set(jnp.arange(token_total, dtype=jnp.int32))
    dealt_queries = queries[source_row].reshape(device_count, row_count, -1)
    shuffled_keys = keys[source_row].reshape(device_count, row_count, -1)
    shuffled_values = values[source_row].reshape(device_count, row_count, -1)
    gathered_rows = jnp.arange(row_count, dtype=jnp.int32)

    def one_device(operands):
        query_rows, key_matrix, value_matrix, request_labels = operands
        token_positions = positions_of(request_labels)
        query_turned = lax.optimization_barrier(apply_rotary(query_rows, token_positions, QUERY_HEAD_COUNT))
        key_turned = lax.optimization_barrier(apply_rotary(key_matrix, token_positions, KEY_VALUE_HEADS))
        output_rows = attend_heads(query_turned, gathered_rows, key_turned, value_matrix, request_labels, KEY_VALUE_HEADS)
        return (output_rows, jnp.concatenate([key_turned, value_matrix], axis=1))
    dealt_out, stored = lax.map(one_device, (dealt_queries, shuffled_keys, shuffled_values, segments))
    attended = dealt_out.reshape(token_total, -1)[deal_index]
    arrival_stored = stored.reshape(token_total, -1)[deal_index]
    page_order = jnp.argsort(page_owner, axis=1).astype(jnp.int32)
    source_page = jnp.arange(device_count, dtype=jnp.int32)[None, :] * device_count + page_order.T
    pages = arrival_stored.reshape(device_count * device_count, page_rows, -1)
    cache = pages[source_page.reshape(-1)].reshape(token_total, -1)
    return (attended, cache)
```

```python
import math

import jax
import jax.numpy as jnp
from jax import lax
from jax.sharding import PartitionSpec as P

QUERY_HEAD_COUNT = 8
KEY_VALUE_HEADS = 4


ROPE_BASE = 100000.0
NEG_FILL = -1e30


def positions_of(request_labels):
    row_width = request_labels.shape[0]
    counter = jnp.arange(row_width, dtype=jnp.int32)
    boundary = jnp.concatenate(
        [jnp.ones((1,), jnp.bool_), request_labels[1:] != request_labels[:-1]]
    )
    starts = lax.cummax(jnp.where(boundary, counter, jnp.zeros_like(counter)), axis=0)
    return counter - starts


def apply_rotary(features, token_positions, head_count):
    head_depth = features.shape[1] // head_count
    half_depth = head_depth // 2
    freqs = ROPE_BASE ** (-2.0 * jnp.arange(half_depth, dtype=jnp.float32) / head_depth)
    angles = token_positions.astype(jnp.float32)[:, None] * freqs[None, :]
    cosine = jnp.cos(angles)[:, None, :]
    sine = jnp.sin(angles)[:, None, :]
    split_heads = features.astype(jnp.float32).reshape(features.shape[0], head_count, head_depth)
    first = split_heads[..., :half_depth]
    second = split_heads[..., half_depth:]
    turned = jnp.concatenate(
        [first * cosine - second * sine, second * cosine + first * sine], axis=-1
    )
    return turned.reshape(features.shape).astype(jnp.bfloat16)


def attend(query_turned, key_turned, value_matrix, allowed, kv_heads):
    rows = query_turned.shape[0]
    head_depth = key_turned.shape[1] // kv_heads
    group_size = query_turned.shape[1] // (kv_heads * head_depth)
    q = query_turned.reshape(rows, kv_heads, group_size, head_depth)
    k = key_turned.reshape(rows, kv_heads, head_depth)
    v = value_matrix.reshape(rows, kv_heads, head_depth)
    logits = jnp.einsum("jhgd,khd->hgjk", q, k, preferred_element_type=jnp.float32)
    logits = logits * (1.0 / math.sqrt(head_depth))
    logits = jnp.where(allowed[None, None], logits, NEG_FILL)
    highest = jnp.max(logits, axis=-1, keepdims=True)
    expo = jnp.exp(logits - highest)
    weights = (expo / jnp.sum(expo, axis=-1, keepdims=True)).astype(jnp.bfloat16)
    out = jnp.einsum("hgjk,khe->jhge", weights, v, preferred_element_type=jnp.float32)
    return out.reshape(rows, -1).astype(jnp.bfloat16)


def row_permute(matrix, target_rows):
    rows = matrix.shape[0]
    onehot = (jnp.arange(rows, dtype=jnp.int32)[:, None] == target_rows[None, :]).astype(
        matrix.dtype
    )
    return jnp.dot(onehot, matrix, preferred_element_type=jnp.float32).astype(matrix.dtype)


def per_device(queries, keys, values, deal_index, segments, page_owner):
    device_count = lax.axis_size("dev")
    row_count = queries.shape[0]
    page_rows = row_count // device_count
    query_width = queries.shape[1]
    key_width = keys.shape[1]
    request_labels = segments[0]
    dealt_positions = positions_of(request_labels)

    arrival_rows = jnp.arange(row_count, dtype=jnp.int32)
    local_dealt = deal_index % row_count
    row_owner = page_owner[0][arrival_rows // page_rows]
    meta = jnp.stack([local_dealt, row_owner], axis=1).astype(jnp.bfloat16)
    outgoing = jnp.concatenate([queries, keys, values, meta], axis=1)
    width = outgoing.shape[1]
    received = lax.all_to_all(
        outgoing.reshape(device_count, page_rows, width), "dev", split_axis=0, concat_axis=0, tiled=True
    ).reshape(row_count, width)

    q_in = received[:, :query_width]
    k_in = received[:, query_width : query_width + key_width]
    v_in = received[:, query_width + key_width : query_width + 2 * key_width]
    dealt_row = received[:, query_width + 2 * key_width].astype(jnp.int32)
    owner_in = received[:, query_width + 2 * key_width + 1].astype(jnp.int32)

    request_in = request_labels[dealt_row]
    position_in = dealt_positions[dealt_row]
    allowed = (request_in[:, None] == request_in[None, :]) & (dealt_row[None, :] <= dealt_row[:, None])

    key_turned = apply_rotary(k_in, position_in, KEY_VALUE_HEADS)
    query_turned = apply_rotary(q_in, position_in, QUERY_HEAD_COUNT)
    output_rows = attend(query_turned, key_turned, v_in, allowed, KEY_VALUE_HEADS)

    source_device = (arrival_rows // page_rows).astype(jnp.bfloat16)[:, None]
    stored = jnp.concatenate([key_turned, v_in, source_device], axis=1)
    stored_for_owner = row_permute(stored, owner_in * page_rows + arrival_rows % page_rows)
    going_back = jnp.concatenate([output_rows, stored_for_owner], axis=1)
    back_width = going_back.shape[1]
    returned = lax.all_to_all(
        going_back.reshape(device_count, page_rows, back_width),
        "dev",
        split_axis=0,
        concat_axis=0,
        tiled=True,
    ).reshape(row_count, back_width)

    attended = returned[:, :query_width]
    cache_in = returned[:, query_width : query_width + 2 * key_width]
    cache_source = returned[:, query_width + 2 * key_width].astype(jnp.int32)
    cache = row_permute(cache_in, cache_source * page_rows + arrival_rows % page_rows)
    return (attended, cache)


def solution(mesh):
    in_specs = (
        P(("grp", "dev"), None),
        P(("grp", "dev"), None),
        P(("grp", "dev"), None),
        P(("grp", "dev")),
        P(("grp", "dev"), None),
        P(("grp", "dev"), None),
    )
    out_specs = (P(("grp", "dev"), None), P(("grp", "dev"), None))
    return jax.shard_map(
        per_device, mesh=mesh, in_specs=in_specs, out_specs=out_specs, check_vma=False
    )
```

```python
import math

import jax
import jax.numpy as jnp
from jax import lax
from jax.sharding import PartitionSpec as P

QUERY_HEAD_COUNT = 8
KEY_VALUE_HEADS = 4


ROPE_BASE = 100000.0
NEG_FILL = -1e30


def positions_of(request_labels):
    row_width = request_labels.shape[0]
    counter = jnp.arange(row_width, dtype=jnp.int32)
    boundary = jnp.concatenate(
        [jnp.ones((1,), jnp.bool_), request_labels[1:] != request_labels[:-1]]
    )
    starts = lax.cummax(jnp.where(boundary, counter, jnp.zeros_like(counter)), axis=0)
    return counter - starts


def apply_rotary(features, token_positions, head_count):
    head_depth = features.shape[1] // head_count
    half_depth = head_depth // 2
    freqs = ROPE_BASE ** (-2.0 * jnp.arange(half_depth, dtype=jnp.float32) / head_depth)
    angles = token_positions.astype(jnp.float32)[:, None] * freqs[None, :]
    cosine = jnp.cos(angles)[:, None, :]
    sine = jnp.sin(angles)[:, None, :]
    split_heads = features.astype(jnp.float32).reshape(features.shape[0], head_count, head_depth)
    first = split_heads[..., :half_depth]
    second = split_heads[..., half_depth:]
    turned = jnp.concatenate(
        [first * cosine - second * sine, second * cosine + first * sine], axis=-1
    )
    return turned.reshape(features.shape).astype(jnp.bfloat16)


def attend(query_turned, key_turned, value_matrix, allowed, kv_heads):
    rows = query_turned.shape[0]
    head_depth = key_turned.shape[1] // kv_heads
    group_size = query_turned.shape[1] // (kv_heads * head_depth)
    q = query_turned.reshape(rows, kv_heads, group_size, head_depth)
    k = key_turned.reshape(rows, kv_heads, head_depth)
    v = value_matrix.reshape(rows, kv_heads, head_depth)
    logits = jnp.einsum("jhgd,khd->hgjk", q, k, preferred_element_type=jnp.float32)
    logits = logits * (1.0 / math.sqrt(head_depth))
    logits = jnp.where(allowed[None, None], logits, NEG_FILL)
    highest = jnp.max(logits, axis=-1, keepdims=True)
    expo = jnp.exp(logits - highest)
    weights = (expo / jnp.sum(expo, axis=-1, keepdims=True)).astype(jnp.bfloat16)
    out = jnp.einsum("hgjk,khe->jhge", weights, v, preferred_element_type=jnp.float32)
    return out.reshape(rows, -1).astype(jnp.bfloat16)


def row_permute(matrix, target_rows):
    rows = matrix.shape[0]
    onehot = (jnp.arange(rows, dtype=jnp.int32)[:, None] == target_rows[None, :]).astype(
        matrix.dtype
    )
    return jnp.dot(onehot, matrix, preferred_element_type=jnp.float32).astype(matrix.dtype)


def one_hot_take(table, index):
    return jnp.sum(
        jnp.where(index[:, None] == jnp.arange(table.shape[0], dtype=jnp.int32)[None, :], table[None, :], 0),
        axis=1,
    )


def row_take(matrix, source_rows):
    rows = matrix.shape[0]
    onehot = (source_rows[:, None] == jnp.arange(rows, dtype=jnp.int32)[None, :]).astype(matrix.dtype)
    return jnp.dot(onehot, matrix, preferred_element_type=jnp.float32).astype(matrix.dtype)


def per_device(queries, keys, values, deal_index, segments, page_owner):
    device_count = lax.axis_size("dev")
    row_count = queries.shape[0]
    page_rows = row_count // device_count
    query_width = queries.shape[1]
    key_width = keys.shape[1]
    request_labels = segments[0]
    dealt_positions = positions_of(request_labels)

    arrival_rows = jnp.arange(row_count, dtype=jnp.int32)
    devices = jnp.arange(device_count, dtype=jnp.int32)
    owner_row = page_owner[0]
    page_of_owner = jnp.sum(
        jnp.where(owner_row[None, :] == devices[:, None], devices[None, :], 0), axis=1
    )
    local_dealt = deal_index % row_count
    page_meta = jnp.where(
        arrival_rows % page_rows == 0,
        jnp.repeat(owner_row, page_rows),
        jnp.repeat(page_of_owner, page_rows),
    )
    meta = jnp.stack([local_dealt, page_meta], axis=1).astype(jnp.bfloat16)
    outgoing = jnp.concatenate([queries, keys, values, meta], axis=1)
    received = lax.all_to_all(outgoing, "dev", split_axis=0, concat_axis=0, tiled=True)

    q_in = received[:, :query_width]
    k_in = received[:, query_width : query_width + key_width]
    v_in = received[:, query_width + key_width : query_width + 2 * key_width]
    dealt_row = received[:, query_width + 2 * key_width].astype(jnp.int32)
    page_meta_in = received[:, query_width + 2 * key_width + 1].astype(jnp.int32)
    paired = page_meta_in.reshape(device_count, page_rows)
    owner_in = jnp.repeat(paired[:, 0], page_rows)
    page_from = jnp.repeat(paired[:, 1], page_rows)

    request_in = one_hot_take(request_labels, dealt_row)
    position_in = one_hot_take(dealt_positions, dealt_row)
    allowed = (request_in[:, None] == request_in[None, :]) & (dealt_row[None, :] <= dealt_row[:, None])

    key_turned = apply_rotary(k_in, position_in, KEY_VALUE_HEADS)
    query_turned = apply_rotary(q_in, position_in, QUERY_HEAD_COUNT)
    output_rows = attend(query_turned, key_turned, v_in, allowed, KEY_VALUE_HEADS)

    stored = jnp.concatenate([key_turned, v_in], axis=1)
    stored_for_owner = row_permute(stored, owner_in * page_rows + arrival_rows % page_rows)
    going_back = jnp.concatenate([output_rows, stored_for_owner], axis=1)
    returned = lax.all_to_all(going_back, "dev", split_axis=0, concat_axis=0, tiled=True)

    attended = returned[:, :query_width]
    cache_in = returned[:, query_width:]
    cache = row_take(cache_in, page_from * page_rows + arrival_rows % page_rows)
    return (attended, cache)


def solution(mesh):
    in_specs = (
        P(("grp", "dev"), None),
        P(("grp", "dev"), None),
        P(("grp", "dev"), None),
        P(("grp", "dev")),
        P(("grp", "dev"), None),
        P(("grp", "dev"), None),
    )
    out_specs = (P(("grp", "dev"), None), P(("grp", "dev"), None))
    return jax.shard_map(
        per_device, mesh=mesh, in_specs=in_specs, out_specs=out_specs, check_vma=False
    )
```

```python
import math

import jax
import jax.numpy as jnp
from jax import lax
from jax.sharding import PartitionSpec as P

QUERY_HEAD_COUNT = 8
KEY_VALUE_HEADS = 4


ROPE_BASE = 100000.0
NEG_FILL = -1e30


def positions_of(request_labels):
    row_width = request_labels.shape[0]
    counter = jnp.arange(row_width, dtype=jnp.int32)
    boundary = jnp.concatenate(
        [jnp.ones((1,), jnp.bool_), request_labels[1:] != request_labels[:-1]]
    )
    starts = lax.cummax(jnp.where(boundary, counter, jnp.zeros_like(counter)), axis=0)
    return counter - starts


def apply_rotary(features, token_positions, head_count):
    head_depth = features.shape[1] // head_count
    half_depth = head_depth // 2
    freqs = ROPE_BASE ** (-2.0 * jnp.arange(half_depth, dtype=jnp.float32) / head_depth)
    angles = token_positions.astype(jnp.float32)[:, None] * freqs[None, :]
    cosine = jnp.cos(angles)[:, None, :]
    sine = jnp.sin(angles)[:, None, :]
    split_heads = features.astype(jnp.float32).reshape(features.shape[0], head_count, head_depth)
    first = split_heads[..., :half_depth]
    second = split_heads[..., half_depth:]
    turned = jnp.concatenate(
        [first * cosine - second * sine, second * cosine + first * sine], axis=-1
    )
    return turned.reshape(features.shape).astype(jnp.bfloat16)


def attend(query_turned, key_turned, value_matrix, allowed, kv_heads):
    rows = query_turned.shape[0]
    head_depth = key_turned.shape[1] // kv_heads
    group_size = query_turned.shape[1] // (kv_heads * head_depth)
    q = query_turned.reshape(rows, kv_heads, group_size, head_depth)
    k = key_turned.reshape(rows, kv_heads, head_depth)
    v = value_matrix.reshape(rows, kv_heads, head_depth)
    logits = jnp.einsum("jhgd,khd->hgjk", q, k, preferred_element_type=jnp.float32)
    logits = logits * (1.0 / math.sqrt(head_depth))
    logits = jnp.where(allowed[None, None], logits, NEG_FILL)
    highest = jnp.max(logits, axis=-1, keepdims=True)
    expo = jnp.exp(logits - highest)
    weights = (expo / jnp.sum(expo, axis=-1, keepdims=True)).astype(jnp.bfloat16)
    out = jnp.einsum("hgjk,khe->jhge", weights, v, preferred_element_type=jnp.float32)
    return out.reshape(rows, -1).astype(jnp.bfloat16)


def row_permute(matrix, target_rows):
    rows = matrix.shape[0]
    onehot = (jnp.arange(rows, dtype=jnp.int32)[:, None] == target_rows[None, :]).astype(
        matrix.dtype
    )
    return jnp.dot(onehot, matrix, preferred_element_type=jnp.float32).astype(matrix.dtype)


def one_hot_take(table, index):
    return jnp.sum(
        jnp.where(index[None, :] == jnp.arange(table.shape[0], dtype=jnp.int32)[:, None], table[:, None], 0),
        axis=0,
    )


def row_take(matrix, source_rows):
    rows = matrix.shape[0]
    onehot = (source_rows[:, None] == jnp.arange(rows, dtype=jnp.int32)[None, :]).astype(matrix.dtype)
    return jnp.dot(onehot, matrix, preferred_element_type=jnp.float32).astype(matrix.dtype)


def per_device(queries, keys, values, deal_index, segments, page_owner):
    device_count = lax.axis_size("dev")
    row_count = queries.shape[0]
    page_rows = row_count // device_count
    query_width = queries.shape[1]
    key_width = keys.shape[1]
    request_labels = segments[0]
    dealt_positions = positions_of(request_labels)

    arrival_rows = jnp.arange(row_count, dtype=jnp.int32)
    devices = jnp.arange(device_count, dtype=jnp.int32)
    owner_row = page_owner[0]
    page_of_owner = jnp.sum(
        jnp.where(owner_row[:, None] == devices[None, :], devices[:, None], 0), axis=0
    )
    local_dealt = (deal_index % row_count).reshape(device_count, page_rows)
    page_meta = jnp.stack([owner_row, page_of_owner], axis=1)
    meta = jnp.stack([local_dealt, page_meta], axis=2).astype(jnp.bfloat16)
    outgoing = jnp.concatenate(
        [part.reshape(device_count, page_rows, -1) for part in (queries, keys, values)] + [meta], axis=2
    )
    received = lax.all_to_all(outgoing, "dev", split_axis=0, concat_axis=0, tiled=True)
    received = received.reshape(row_count, -1)

    q_in = received[:, :query_width]
    k_in = received[:, query_width : query_width + key_width]
    v_in = received[:, query_width + key_width : query_width + 2 * key_width]
    dealt_row = received[:, query_width + 2 * key_width].astype(jnp.int32)
    page_meta_in = received[:, query_width + 2 * key_width + 1].astype(jnp.int32)
    paired = page_meta_in.reshape(device_count, page_rows)
    owner_in = jnp.repeat(paired[:, 0], page_rows)
    page_from = jnp.repeat(paired[:, 1], page_rows)

    request_in = one_hot_take(request_labels, dealt_row)
    position_in = one_hot_take(dealt_positions, dealt_row)
    allowed = (request_in[:, None] == request_in[None, :]) & (dealt_row[None, :] <= dealt_row[:, None])

    key_turned = apply_rotary(k_in, position_in, KEY_VALUE_HEADS)
    query_turned = apply_rotary(q_in, position_in, QUERY_HEAD_COUNT)
    output_rows = attend(query_turned, key_turned, v_in, allowed, KEY_VALUE_HEADS)

    stored = jnp.concatenate([key_turned, v_in], axis=1)
    stored_for_owner = row_permute(stored, owner_in * page_rows + arrival_rows % page_rows)
    going_back = jnp.concatenate([output_rows, stored_for_owner], axis=1)
    returned = lax.all_to_all(going_back, "dev", split_axis=0, concat_axis=0, tiled=True)

    attended = returned[:, :query_width]
    cache_in = returned[:, query_width:]
    cache = row_take(cache_in, page_from * page_rows + arrival_rows % page_rows)
    return (attended, cache)


def solution(mesh):
    in_specs = (
        P(("grp", "dev"), None),
        P(("grp", "dev"), None),
        P(("grp", "dev"), None),
        P(("grp", "dev")),
        P(("grp", "dev"), None),
        P(("grp", "dev"), None),
    )
    out_specs = (P(("grp", "dev"), None), P(("grp", "dev"), None))
    return jax.shard_map(
        per_device, mesh=mesh, in_specs=in_specs, out_specs=out_specs, check_vma=False
    )
```

```python
import math

import jax
import jax.numpy as jnp
from jax import lax
from jax.experimental import pallas as pl
from jax.sharding import PartitionSpec as P

QUERY_HEAD_COUNT = 8
KEY_VALUE_HEADS = 4


ROPE_BASE = 100000.0
NEG_FILL = -1e30


def positions_of(request_labels):
    row_width = request_labels.shape[0]
    counter = jnp.arange(row_width, dtype=jnp.int32)
    boundary = jnp.concatenate(
        [jnp.ones((1,), jnp.bool_), request_labels[1:] != request_labels[:-1]]
    )
    starts = lax.cummax(jnp.where(boundary, counter, jnp.zeros_like(counter)), axis=0)
    return counter - starts


def apply_rotary(features, token_positions, head_count):
    head_depth = features.shape[1] // head_count
    half_depth = head_depth // 2
    freqs = ROPE_BASE ** (-2.0 * jnp.arange(half_depth, dtype=jnp.float32) / head_depth)
    angles = token_positions.astype(jnp.float32)[:, None] * freqs[None, :]
    cosine = jnp.cos(angles)[:, None, :]
    sine = jnp.sin(angles)[:, None, :]
    split_heads = features.astype(jnp.float32).reshape(features.shape[0], head_count, head_depth)
    first = split_heads[..., :half_depth]
    second = split_heads[..., half_depth:]
    turned = jnp.concatenate(
        [first * cosine - second * sine, second * cosine + first * sine], axis=-1
    )
    return turned.reshape(features.shape).astype(jnp.bfloat16)


def attend(query_turned, key_turned, value_matrix, allowed, kv_heads):
    rows = query_turned.shape[0]
    head_depth = key_turned.shape[1] // kv_heads
    group_size = query_turned.shape[1] // (kv_heads * head_depth)
    q = query_turned.reshape(rows, kv_heads, group_size, head_depth)
    k = key_turned.reshape(rows, kv_heads, head_depth)
    v = value_matrix.reshape(rows, kv_heads, head_depth)
    logits = jnp.einsum("jhgd,khd->hgjk", q, k, preferred_element_type=jnp.float32)
    logits = logits * (1.0 / math.sqrt(head_depth))
    logits = jnp.where(allowed[None, None], logits, NEG_FILL)
    highest = jnp.max(logits, axis=-1, keepdims=True)
    expo = jnp.exp(logits - highest)
    weights = (expo / jnp.sum(expo, axis=-1, keepdims=True)).astype(jnp.bfloat16)
    out = jnp.einsum("hgjk,khe->jhge", weights, v, preferred_element_type=jnp.float32)
    return out.reshape(rows, -1).astype(jnp.bfloat16)


NT = (((1,), (1,)), ((), ()))


def _pack_kernel(q_ref, k_ref, v_ref, d_ref, o_ref, out_ref):
    rows = q_ref.shape[0]
    pages = o_ref.shape[1]
    page_rows = rows // pages
    qw, kw = q_ref.shape[1], k_ref.shape[1]
    owner = o_ref[...]
    o_iota = lax.broadcasted_iota(jnp.int32, (pages, pages), 0)
    p_iota = lax.broadcasted_iota(jnp.int32, (pages, pages), 1)
    hits = (owner == o_iota).astype(jnp.bfloat16)
    page_numbers = lax.broadcasted_iota(jnp.int32, (8, pages), 1).astype(jnp.bfloat16)
    page_of_owner = lax.dot_general(page_numbers, hits, NT, preferred_element_type=jnp.float32)[0:1]
    dealt = (d_ref[...] % rows).astype(jnp.float32)
    width = rows + 2 * pages
    src_row = lax.broadcasted_iota(jnp.int32, (128, width), 0)
    src_col = lax.broadcasted_iota(jnp.int32, (128, width), 1)
    dealt_ext = jnp.concatenate([dealt, jnp.zeros((1, 2 * pages), jnp.float32)], axis=1)
    page_ext = jnp.concatenate(
        [jnp.zeros((1, rows), jnp.float32), owner.astype(jnp.float32), page_of_owner], axis=1
    )
    sources = jnp.where(src_row == 0, dealt_ext, jnp.where(src_row == 1, page_ext, 0.0)).astype(jnp.bfloat16)
    i = lax.broadcasted_iota(jnp.int32, (rows, width), 0)
    m = lax.broadcasted_iota(jnp.int32, (rows, width), 1)
    even = i % page_rows == 0
    spread = (
        (m == i)
        | ((m - rows == i // page_rows) & even)
        | ((m - rows - pages == i // page_rows) & ~even)
    ).astype(jnp.bfloat16)
    meta = lax.dot_general(spread, sources, NT, preferred_element_type=jnp.float32)
    out_ref[:, 0:qw] = q_ref[...]
    out_ref[:, qw : qw + kw] = k_ref[...]
    out_ref[:, qw + kw : qw + 2 * kw] = v_ref[...]
    out_ref[:, qw + 2 * kw :] = meta.astype(jnp.bfloat16)


def pack_outgoing(queries, keys, values, deal_index, page_owner):
    rows = queries.shape[0]
    width = queries.shape[1] + 2 * keys.shape[1] + 128
    return pl.pallas_call(
        _pack_kernel,
        out_shape=jax.ShapeDtypeStruct((rows, width), queries.dtype),
    )(queries, keys, values, deal_index.reshape(1, rows), page_owner)


def row_permute(matrix, target_rows):
    rows = matrix.shape[0]
    onehot = (jnp.arange(rows, dtype=jnp.int32)[:, None] == target_rows[None, :]).astype(
        matrix.dtype
    )
    return jnp.dot(onehot, matrix, preferred_element_type=jnp.float32).astype(matrix.dtype)


def one_hot_take(table, index):
    return jnp.sum(
        jnp.where(index[:, None] == jnp.arange(table.shape[0], dtype=jnp.int32)[None, :], table[None, :], 0),
        axis=1,
    )


def row_take(matrix, source_rows):
    rows = matrix.shape[0]
    onehot = (source_rows[:, None] == jnp.arange(rows, dtype=jnp.int32)[None, :]).astype(matrix.dtype)
    return jnp.dot(onehot, matrix, preferred_element_type=jnp.float32).astype(matrix.dtype)


def per_device(queries, keys, values, deal_index, segments, page_owner):
    device_count = lax.axis_size("dev")
    row_count = queries.shape[0]
    page_rows = row_count // device_count
    query_width = queries.shape[1]
    key_width = keys.shape[1]
    request_labels = segments[0]
    dealt_positions = positions_of(request_labels)

    arrival_rows = jnp.arange(row_count, dtype=jnp.int32)
    outgoing = pack_outgoing(queries, keys, values, deal_index, page_owner)
    received = lax.all_to_all(outgoing, "dev", split_axis=0, concat_axis=0, tiled=True)

    q_in = received[:, :query_width]
    k_in = received[:, query_width : query_width + key_width]
    v_in = received[:, query_width + key_width : query_width + 2 * key_width]
    dealt_row = received[:, query_width + 2 * key_width].astype(jnp.int32)
    page_meta_in = received[:, query_width + 2 * key_width + 1].astype(jnp.int32)
    paired = page_meta_in.reshape(device_count, page_rows)
    owner_in = jnp.repeat(paired[:, 0], page_rows)
    page_from = jnp.repeat(paired[:, 1], page_rows)

    request_in = one_hot_take(request_labels, dealt_row)
    position_in = one_hot_take(dealt_positions, dealt_row)
    allowed = (request_in[:, None] == request_in[None, :]) & (dealt_row[None, :] <= dealt_row[:, None])

    key_turned = apply_rotary(k_in, position_in, KEY_VALUE_HEADS)
    query_turned = apply_rotary(q_in, position_in, QUERY_HEAD_COUNT)
    output_rows = attend(query_turned, key_turned, v_in, allowed, KEY_VALUE_HEADS)

    stored = jnp.concatenate([key_turned, v_in], axis=1)
    stored_for_owner = row_permute(stored, owner_in * page_rows + arrival_rows % page_rows)
    going_back = jnp.concatenate([output_rows, stored_for_owner], axis=1)
    returned = lax.all_to_all(going_back, "dev", split_axis=0, concat_axis=0, tiled=True)

    attended = returned[:, :query_width]
    cache_in = returned[:, query_width:]
    cache = row_take(cache_in, page_from * page_rows + arrival_rows % page_rows)
    return (attended, cache)


def solution(mesh):
    in_specs = (
        P(("grp", "dev"), None),
        P(("grp", "dev"), None),
        P(("grp", "dev"), None),
        P(("grp", "dev")),
        P(("grp", "dev"), None),
        P(("grp", "dev"), None),
    )
    out_specs = (P(("grp", "dev"), None), P(("grp", "dev"), None))
    return jax.shard_map(
        per_device, mesh=mesh, in_specs=in_specs, out_specs=out_specs, check_vma=False
    )
```

```python
import math

import jax
import jax.numpy as jnp
from jax import lax
from jax.experimental import pallas as pl
from jax.sharding import PartitionSpec as P

QUERY_HEAD_COUNT = 8
KEY_VALUE_HEADS = 4


ROPE_BASE = 100000.0
NEG_FILL = -1e30


def positions_of(request_labels):
    row_width = request_labels.shape[0]
    counter = jnp.arange(row_width, dtype=jnp.int32)
    boundary = jnp.concatenate(
        [jnp.ones((1,), jnp.bool_), request_labels[1:] != request_labels[:-1]]
    )
    starts = lax.cummax(jnp.where(boundary, counter, jnp.zeros_like(counter)), axis=0)
    return counter - starts


def apply_rotary(features, token_positions, head_count):
    head_depth = features.shape[1] // head_count
    half_depth = head_depth // 2
    freqs = ROPE_BASE ** (-2.0 * jnp.arange(half_depth, dtype=jnp.float32) / head_depth)
    angles = token_positions.astype(jnp.float32)[:, None] * freqs[None, :]
    cosine = jnp.cos(angles)[:, None, :]
    sine = jnp.sin(angles)[:, None, :]
    split_heads = features.astype(jnp.float32).reshape(features.shape[0], head_count, head_depth)
    first = split_heads[..., :half_depth]
    second = split_heads[..., half_depth:]
    turned = jnp.concatenate(
        [first * cosine - second * sine, second * cosine + first * sine], axis=-1
    )
    return turned.reshape(features.shape).astype(jnp.bfloat16)


def attend(query_turned, key_turned, value_matrix, allowed, kv_heads):
    rows = query_turned.shape[0]
    head_depth = key_turned.shape[1] // kv_heads
    group_size = query_turned.shape[1] // (kv_heads * head_depth)
    q = query_turned.reshape(rows, kv_heads, group_size, head_depth)
    k = key_turned.reshape(rows, kv_heads, head_depth)
    v = value_matrix.reshape(rows, kv_heads, head_depth)
    logits = jnp.einsum("jhgd,khd->hgjk", q, k, preferred_element_type=jnp.float32)
    logits = logits * (1.0 / math.sqrt(head_depth))
    logits = jnp.where(allowed[None, None], logits, NEG_FILL)
    highest = jnp.max(logits, axis=-1, keepdims=True)
    expo = jnp.exp(logits - highest)
    weights = (expo / jnp.sum(expo, axis=-1, keepdims=True)).astype(jnp.bfloat16)
    out = jnp.einsum("hgjk,khe->jhge", weights, v, preferred_element_type=jnp.float32)
    return out.reshape(rows, -1).astype(jnp.bfloat16)


NT = (((1,), (1,)), ((), ()))


def _pack_kernel(d_ref, o_ref, out_ref):
    rows = d_ref.shape[1]
    pages = o_ref.shape[1]
    page_rows = rows // pages
    owner = o_ref[...]
    o_iota = lax.broadcasted_iota(jnp.int32, (pages, pages), 0)
    p_iota = lax.broadcasted_iota(jnp.int32, (pages, pages), 1)
    hits = (owner == o_iota).astype(jnp.bfloat16)
    page_numbers = lax.broadcasted_iota(jnp.int32, (8, pages), 1).astype(jnp.bfloat16)
    page_of_owner = lax.dot_general(page_numbers, hits, NT, preferred_element_type=jnp.float32)[0:1]
    dealt = (d_ref[...] % rows).astype(jnp.float32)
    width = rows + 2 * pages
    src_row = lax.broadcasted_iota(jnp.int32, (128, width), 0)
    src_col = lax.broadcasted_iota(jnp.int32, (128, width), 1)
    dealt_ext = jnp.concatenate([dealt, jnp.zeros((1, 2 * pages), jnp.float32)], axis=1)
    page_ext = jnp.concatenate(
        [jnp.zeros((1, rows), jnp.float32), owner.astype(jnp.float32), page_of_owner], axis=1
    )
    sources = jnp.where(src_row == 0, dealt_ext, jnp.where(src_row == 1, page_ext, 0.0)).astype(jnp.bfloat16)
    i = lax.broadcasted_iota(jnp.int32, (rows, width), 0)
    m = lax.broadcasted_iota(jnp.int32, (rows, width), 1)
    even = i % page_rows == 0
    spread = (
        (m == i)
        | ((m - rows == i // page_rows) & even)
        | ((m - rows - pages == i // page_rows) & ~even)
    ).astype(jnp.bfloat16)
    meta = lax.dot_general(spread, sources, NT, preferred_element_type=jnp.float32)
    out_ref[...] = meta.astype(jnp.bfloat16)


def pack_outgoing(queries, keys, values, deal_index, page_owner):
    rows = queries.shape[0]
    meta = pl.pallas_call(
        _pack_kernel,
        out_shape=jax.ShapeDtypeStruct((rows, 128), queries.dtype),
    )(deal_index.reshape(1, rows), page_owner)
    return jnp.concatenate([queries, keys, values, meta], axis=1)


def row_permute(matrix, target_rows):
    rows = matrix.shape[0]
    onehot = (jnp.arange(rows, dtype=jnp.int32)[:, None] == target_rows[None, :]).astype(
        matrix.dtype
    )
    return jnp.dot(onehot, matrix, preferred_element_type=jnp.float32).astype(matrix.dtype)


def one_hot_take(table, index):
    return jnp.sum(
        jnp.where(index[:, None] == jnp.arange(table.shape[0], dtype=jnp.int32)[None, :], table[None, :], 0),
        axis=1,
    )


def row_take(matrix, source_rows):
    rows = matrix.shape[0]
    onehot = (source_rows[:, None] == jnp.arange(rows, dtype=jnp.int32)[None, :]).astype(matrix.dtype)
    return jnp.dot(onehot, matrix, preferred_element_type=jnp.float32).astype(matrix.dtype)


def per_device(queries, keys, values, deal_index, segments, page_owner):
    device_count = lax.axis_size("dev")
    row_count = queries.shape[0]
    page_rows = row_count // device_count
    query_width = queries.shape[1]
    key_width = keys.shape[1]
    request_labels = segments[0]
    dealt_positions = positions_of(request_labels)

    arrival_rows = jnp.arange(row_count, dtype=jnp.int32)
    outgoing = pack_outgoing(queries, keys, values, deal_index, page_owner)
    received = lax.all_to_all(outgoing, "dev", split_axis=0, concat_axis=0, tiled=True)

    q_in = received[:, :query_width]
    k_in = received[:, query_width : query_width + key_width]
    v_in = received[:, query_width + key_width : query_width + 2 * key_width]
    dealt_row = received[:, query_width + 2 * key_width].astype(jnp.int32)
    page_meta_in = received[:, query_width + 2 * key_width + 1].astype(jnp.int32)
    paired = page_meta_in.reshape(device_count, page_rows)
    owner_in = jnp.repeat(paired[:, 0], page_rows)
    page_from = jnp.repeat(paired[:, 1], page_rows)

    request_in = one_hot_take(request_labels, dealt_row)
    position_in = one_hot_take(dealt_positions, dealt_row)
    allowed = (request_in[:, None] == request_in[None, :]) & (dealt_row[None, :] <= dealt_row[:, None])

    key_turned = apply_rotary(k_in, position_in, KEY_VALUE_HEADS)
    query_turned = apply_rotary(q_in, position_in, QUERY_HEAD_COUNT)
    output_rows = attend(query_turned, key_turned, v_in, allowed, KEY_VALUE_HEADS)

    stored = jnp.concatenate([key_turned, v_in], axis=1)
    stored_for_owner = row_permute(stored, owner_in * page_rows + arrival_rows % page_rows)
    going_back = jnp.concatenate([output_rows, stored_for_owner], axis=1)
    returned = lax.all_to_all(going_back, "dev", split_axis=0, concat_axis=0, tiled=True)

    attended = returned[:, :query_width]
    cache_in = returned[:, query_width:]
    cache = row_take(cache_in, page_from * page_rows + arrival_rows % page_rows)
    return (attended, cache)


def solution(mesh):
    in_specs = (
        P(("grp", "dev"), None),
        P(("grp", "dev"), None),
        P(("grp", "dev"), None),
        P(("grp", "dev")),
        P(("grp", "dev"), None),
        P(("grp", "dev"), None),
    )
    out_specs = (P(("grp", "dev"), None), P(("grp", "dev"), None))
    return jax.shard_map(
        per_device, mesh=mesh, in_specs=in_specs, out_specs=out_specs, check_vma=False
    )
```
